256 devices in a mesh: dp: 16 (over z, x_lo), own: 16 (over x_hi, y, core).
Axes of the slice: x: 4 (x_hi: 2, x_lo: 2; x = x_hi * 2 + x_lo), y: 4, z: 8, core: 2. Of those that a mesh axis runs over, the one named last changes fastest.
Arguments:
- grads: float32 [16, 16, 1024, 1024], P('dp', None, 'own'), may hold values from -0.27 to 0.27
- owner_map: int32 [16], replicated, may hold values from 0 to 31, as said below
- stat_left: float32 [32, 1024, 1024], P('own', 'dp'), as said below
- stat_right: float32 [32, 1024, 1024], P('own', 'dp'), as said below
- root_left: bfloat16 [32, 1024, 1024], P('own', 'dp'), as said below
- root_right: bfloat16 [32, 1024, 1024], P('own', 'dp'), as said below
- master: float32 [32, 1024, 1024], P('own', 'dp'), may hold values from -4 to 4
- moment_first: float32 [32, 1024, 1024], P('own', 'dp'), may hold values from -0.6 to 0.6
- moment_second: float32 [32, 1024, 1024], P('own', 'dp'), may hold values from 0.001 to 1, as said below
Outputs:
- left_next: float32 [32, 1024, 1024], P('own', 'dp')
- right_next: float32 [32, 1024, 1024], P('own', 'dp')
- master_next: float32 [32, 1024, 1024], P('own', 'dp')
- first_next: float32 [32, 1024, 1024], P('own', 'dp')
- second_next: float32 [32, 1024, 1024], P('own', 'dp')
- weights_out: bfloat16 [16, 1024, 1024], P(None, ('dp', 'own'))
The draws below stay inside these ranges and needn't reach their ends.
Inputs may be any that keep to these rules, and one draw needn't show every extreme that they name: `owner_map`: no two blocks share a slot. In every draw all 2 slots of some owner are taken, and so are slots 0 and 31. `root_left`: symmetric in its last two dimensions. `root_right`: symmetric in its last two dimensions. `stat_left`: symmetric in its last two dimensions. `stat_right`: symmetric in its last two dimensions. `moment_second`: Positive.
All inputs are finite; a program needn't handle non-finite values.
Results may differ from the reference program's by a relative error of at most 0.0045.
Values may be sent and summed in bfloat16 or wider, within the bound.
No kernel may reach another device: no remote copies, remote signals or barrier semaphores. Data moves between devices by JAX's collectives and lax.ppermute only.
A program may use at most 128 MiB of HBM per device.

```python
import jax
import jax.numpy as jnp
from jax import lax

B = 1024
SLOTS = 2
BLOCKS = 16
OWNED = 32
GROUPS = 16


def symmetric_blocks(key, exponent):
    normals = jax.random.normal(jax.random.fold_in(key, 11), (OWNED, B, B), jnp.float32)
    symmetric = (normals + jnp.swapaxes(normals, 1, 2)) * 0.5 ** 0.5 / B ** 0.5
    diagonal = jax.random.uniform(jax.random.fold_in(key, 12), (OWNED, B), jnp.float32, 1.0, 2.0)
    identity = (jnp.arange(B)[:, None] == jnp.arange(B)[None, :]).astype(jnp.float32)
    matrix = symmetric + identity[None, :, :] * diagonal[:, :, None]
    position = jnp.arange(B, dtype=jnp.float32) / B
    row_scale = 10.0 ** (exponent * position)
    return matrix * row_scale[None, :, None] * row_scale[None, None, :]


def draw_owner_map(key, part):
    busiest = jax.random.randint(jax.random.fold_in(key, 21), (), 0, OWNED // SLOTS)
    priority = jax.random.permutation(jax.random.fold_in(key, 22), OWNED).astype(jnp.int32)
    indices = jnp.arange(OWNED, dtype=jnp.int32)
    forced = (indices == 0) | (indices == OWNED - 1) | (indices // SLOTS == busiest)
    scores = priority + OWNED * forced.astype(jnp.int32)
    ordering = jnp.argsort(-scores, stable=True).astype(jnp.int32)
    chosen = ordering[:BLOCKS]
    shuffle = jax.random.permutation(jax.random.fold_in(key, 23), BLOCKS)
    return chosen[shuffle].astype(jnp.int32)


def draw_stat_left(key, part):
    return symmetric_blocks(jax.random.fold_in(key, 31), 0.0)


def draw_stat_right(key, part):
    return symmetric_blocks(jax.random.fold_in(key, 32), 0.0)


def draw_root_left(key, part):
    return symmetric_blocks(jax.random.fold_in(key, 33), 1.0).astype(jnp.bfloat16)


def draw_root_right(key, part):
    return symmetric_blocks(jax.random.fold_in(key, 34), 0.5).astype(jnp.bfloat16)


def draw_moment_second(key, part):
    uniforms = jax.random.uniform(jax.random.fold_in(key, 35), (OWNED, B, B), jnp.float32)
    position = jnp.arange(B, dtype=jnp.float32) / B
    return 0.001 * 10.0 ** (uniforms + 2.0 * position[None, :, None])


def spiked(values, rng, source, target, blocks, factor):
    owner, partner = [(jnp.arange(values.shape[dim]) // (values.shape[dim] // blocks)).reshape([-1 if axis == dim else 1 for axis in range(values.ndim)]) for dim in (source, target)]
    chosen = jax.random.permutation(rng, blocks)[partner]
    strong = (owner == chosen) | (owner == (partner + blocks // 2) % blocks)
    return jnp.where(strong, factor * values, values)


def block_levels(own_key, dims, cuts, least, high):
    def one(dim, blocks):
        draws = jax.random.uniform(jax.random.fold_in(jax.random.fold_in(own_key, 6), dim), (blocks,), jnp.float32, least / len(cuts), high / len(cuts))
        return jnp.repeat(jnp.exp(draws), dims[dim] // blocks).reshape((-1,) + (1,) * (len(dims) - dim - 1))

    level = one(*cuts[0])
    for cut in cuts[1:]:
        level = level * one(*cut)
    return level


def bell_draw(own_key, dims, deviation, limit, cuts=(), kind=jnp.bfloat16):
    values = deviation * jax.random.normal(own_key, dims, jnp.float32)
    if cuts:
        values = values * block_levels(own_key, dims, cuts, -0.22, 0.18)
    return jnp.clip(values, -limit, limit).astype(kind)


def bell_draw_with(own_key, shape, scale, reach, shards, heavy, kind=jnp.bfloat16):
    array = scale * jax.random.normal(own_key, shape, jnp.float32)
    if shards:
        array = array * block_levels(own_key, shape, shards, -0.22, 0.18)
    return jnp.clip(spiked(array, jax.random.fold_in(own_key, 3), *heavy), -reach, reach).astype(kind)


def setup_inputs(seed: int = 0) -> dict:
    key_of = jax.random.split(jax.random.key(seed), 10)
    grads = bell_draw_with(key_of[0], (GROUPS, BLOCKS, B, B), 0.045, 0.27, ((0, 16), (2, 16)), (0, 2, 16, 2.0), jnp.float32)
    owner_map = draw_owner_map(jax.random.fold_in(key_of[9], 71), 0)
    stat_left = draw_stat_left(jax.random.fold_in(key_of[9], 71), 0)
    stat_right = draw_stat_right(jax.random.fold_in(key_of[9], 71), 0)
    root_left = draw_root_left(jax.random.fold_in(key_of[9], 71), 0)
    root_right = draw_root_right(jax.random.fold_in(key_of[9], 71), 0)
    master = bell_draw(key_of[6], (OWNED, B, B), 1.0, 4.0, ((0, 16), (1, 16)), jnp.float32)
    moment_first = bell_draw(key_of[7], (OWNED, B, B), 0.1, 0.6, ((0, 16), (1, 16)), jnp.float32)
    moment_second = draw_moment_second(jax.random.fold_in(key_of[9], 71), 0)
    return dict(grads=grads, owner_map=owner_map, stat_left=stat_left, stat_right=stat_right, root_left=root_left, root_right=root_right, master=master, moment_first=moment_first, moment_second=moment_second)


stat_decay = 0.9
first_decay = 0.9
second_decay = 0.99
learn_rate = 0.25

def refresh(block_items):
    gradient, left_stat, right_stat, root_left, root_right, weight, first_moment, second_moment = block_items
    highest = lax.Precision.HIGHEST
    left_next = stat_decay * left_stat + (1.0 - stat_decay) * jnp.dot(gradient, gradient.T, precision=highest, preferred_element_type=jnp.float32)
    right_next = stat_decay * right_stat + (1.0 - stat_decay) * jnp.dot(gradient.T, gradient, precision=highest, preferred_element_type=jnp.float32)
    first_next = first_decay * first_moment + (1.0 - first_decay) * gradient
    second_next = second_decay * second_moment + (1.0 - second_decay) * gradient * gradient
    adam_step = first_next / (jnp.sqrt(second_next) + 1e-08)
    product = jnp.dot(gradient.astype(jnp.bfloat16), root_right, preferred_element_type=jnp.float32).astype(jnp.bfloat16)
    direction = jnp.dot(root_left, product, preferred_element_type=jnp.float32)
    graft = jnp.sqrt(jnp.sum(adam_step * adam_step)) / (jnp.sqrt(jnp.sum(direction * direction)) + 1e-06)
    weight_next = weight - learn_rate * graft * direction
    return (left_next, right_next, weight_next, first_next, second_next)

def reference(grads, owner_map, stat_left, stat_right, root_left, root_right, master, moment_first, moment_second):
    summed = lax.optimization_barrier(jnp.sum(grads, axis=0))
    picked = tuple((jnp.take(states, owner_map, axis=0) for states in (stat_left, stat_right, root_left, root_right, master, moment_first, moment_second)))
    results = lax.map(refresh, (summed,) + picked)
    befores = (stat_left, stat_right, master, moment_first, moment_second)
    updated = tuple((before.at[owner_map].set(after) for before, after in zip(befores, results)))
    weights_out = results[2].astype(jnp.bfloat16)
    return (updated[0], updated[1], updated[2], updated[3], updated[4], weights_out)
```

```python
import jax
import jax.numpy as jnp
from jax import lax
from jax.sharding import PartitionSpec as P

stat_decay = 0.9
first_decay = 0.9
second_decay = 0.99
learn_rate = 0.25


def per_device(
    grads,
    owner_map,
    stat_left,
    stat_right,
    root_left,
    root_right,
    master,
    moment_first,
    moment_second,
):
    owners = lax.axis_size("own")
    slot_count = stat_left.shape[0]
    rows_dev = stat_left.shape[1]
    order_size = stat_left.shape[2]
    blocks = owner_map.shape[0]
    owned_slots = owners * slot_count
    matches = owner_map[:, None] == jnp.arange(owned_slots, dtype=jnp.int32)[None, :]
    occupied = jnp.any(matches, axis=0)
    block_of = jnp.sum(jnp.where(matches, jnp.arange(blocks, dtype=jnp.int32)[:, None], 0), axis=0)
    partials = grads[0]
    summed = lax.psum(partials, "dp")
    packed = jnp.where(occupied[:, None, None], jnp.take(summed, block_of, axis=0), 0.0)
    packed = packed.reshape(owners, slot_count, summed.shape[1], order_size)
    arrived = lax.all_to_all(
        packed.astype(jnp.bfloat16), "own", split_axis=0, concat_axis=2, tiled=True
    )
    right_full = lax.all_gather(root_right, "dp", axis=1, tiled=True)
    first_row = lax.axis_index("dp") * rows_dev
    rounded = arrived.reshape(slot_count, order_size, order_size)
    row_part = lax.dynamic_slice_in_dim(rounded, first_row, rows_dev, 1)
    col_part = lax.dynamic_slice_in_dim(rounded, first_row, rows_dev, 2)
    own_rows = row_part.astype(jnp.float32)
    left_new = stat_decay * stat_left + (1.0 - stat_decay) * jnp.einsum(
        "srk,snk->srn", row_part, rounded, preferred_element_type=jnp.float32
    )
    right_new = stat_decay * stat_right + (1.0 - stat_decay) * jnp.einsum(
        "skr,skn->srn", col_part, rounded, preferred_element_type=jnp.float32
    )
    first_new = first_decay * moment_first + (1.0 - first_decay) * own_rows
    second_new = second_decay * moment_second + (1.0 - second_decay) * own_rows * own_rows
    adam_step = first_new / (jnp.sqrt(second_new) + 1e-08)
    product = jnp.einsum(
        "skn,snr->skr", rounded, right_full, preferred_element_type=jnp.float32
    ).astype(jnp.bfloat16)
    direction = jnp.einsum(
        "srk,skn->srn", root_left, product, preferred_element_type=jnp.float32
    )
    square_sums = lax.psum(
        (jnp.sum(adam_step * adam_step, axis=(1, 2)), jnp.sum(direction * direction, axis=(1, 2))),
        "dp",
    )
    graft = jnp.sqrt(square_sums[0]) / (jnp.sqrt(square_sums[1]) + 1e-06)
    master_new = master - learn_rate * graft[:, None, None] * direction
    occupied_mine = lax.dynamic_slice_in_dim(
        occupied, lax.axis_index("own") * slot_count, slot_count
    )[:, None, None]
    left_next = jnp.where(occupied_mine, left_new, stat_left)
    right_next = jnp.where(occupied_mine, right_new, stat_right)
    master_next = jnp.where(occupied_mine, master_new, master)
    first_next = jnp.where(occupied_mine, first_new, moment_first)
    second_next = jnp.where(occupied_mine, second_new, moment_second)
    shares = master_new.astype(jnp.bfloat16).reshape(
        slot_count, owners, rows_dev // owners, order_size
    )
    delivered = lax.all_to_all(shares, "own", split_axis=1, concat_axis=0, tiled=True)
    delivered = delivered.reshape(owned_slots, rows_dev // owners, order_size)
    weights_out = jnp.take(delivered, owner_map, axis=0)
    return (left_next, right_next, master_next, first_next, second_next, weights_out)


def solution(mesh):
    return jax.shard_map(
        per_device,
        mesh=mesh,
        in_specs=(
            P("dp", None, "own", None),
            P(),
            P("own", "dp", None),
            P("own", "dp", None),
            P("own", "dp", None),
            P("own", "dp", None),
            P("own", "dp", None),
            P("own", "dp", None),
            P("own", "dp", None),
        ),
        out_specs=(
            P("own", "dp", None),
            P("own", "dp", None),
            P("own", "dp", None),
            P("own", "dp", None),
            P("own", "dp", None),
            P(None, ("dp", "own"), None),
        ),
        check_vma=False,
    )
```

```python
import jax
import jax.numpy as jnp
from jax import lax
from jax.sharding import Mesh, PartitionSpec as P

stat_decay = 0.9
first_decay = 0.9
second_decay = 0.99
learn_rate = 0.25
DP = ("z", "xlo")


def dp_index():
    return lax.axis_index("z") * lax.axis_size("xlo") + lax.axis_index("xlo")


def dp_gather(x, axis):
    x = lax.all_gather(x, "xlo", axis=axis, tiled=True)
    return lax.all_gather(x, "z", axis=axis, tiled=True)


def dp_sum(x):
    x = lax.psum_scatter(x, "xlo", scatter_dimension=1, tiled=True)
    x = lax.psum(x, "z")
    return lax.all_gather(x, "xlo", axis=1, tiled=True)


def per_device(
    grads,
    owner_map,
    stat_left,
    stat_right,
    root_left,
    root_right,
    master,
    moment_first,
    moment_second,
):
    owners = lax.axis_size("own")
    slot_count = stat_left.shape[0]
    rows_dev = stat_left.shape[1]
    order_size = stat_left.shape[2]
    blocks = owner_map.shape[0]
    owned_slots = owners * slot_count
    matches = owner_map[:, None] == jnp.arange(owned_slots, dtype=jnp.int32)[None, :]
    occupied = jnp.any(matches, axis=0)
    block_of = jnp.sum(jnp.where(matches, jnp.arange(blocks, dtype=jnp.int32)[:, None], 0), axis=0)
    summed = dp_sum(grads[0].astype(jnp.bfloat16))
    summed, root_right = lax.optimization_barrier((summed, root_right))
    packed = jnp.where(occupied[:, None, None], jnp.take(summed, block_of, axis=0), 0.0)
    packed = packed.reshape(owners, slot_count, summed.shape[1], order_size)
    arrived = lax.all_to_all(packed, "own", split_axis=0, concat_axis=2, tiled=True)
    right_full = dp_gather(root_right, 1)
    first_row = dp_index() * rows_dev
    rounded = arrived.reshape(slot_count, order_size, order_size)
    row_part = lax.dynamic_slice_in_dim(rounded, first_row, rows_dev, 1)
    col_part = lax.dynamic_slice_in_dim(rounded, first_row, rows_dev, 2)
    own_rows = row_part.astype(jnp.float32)
    left_new = stat_decay * stat_left + (1.0 - stat_decay) * jnp.einsum(
        "srk,snk->srn", row_part, rounded, preferred_element_type=jnp.float32
    )
    right_new = stat_decay * stat_right + (1.0 - stat_decay) * jnp.einsum(
        "skr,skn->srn", col_part, rounded, preferred_element_type=jnp.float32
    )
    first_new = first_decay * moment_first + (1.0 - first_decay) * own_rows
    second_new = second_decay * moment_second + (1.0 - second_decay) * own_rows * own_rows
    adam_step = first_new / (jnp.sqrt(second_new) + 1e-08)
    product = jnp.einsum(
        "skn,snr->skr", rounded, right_full, preferred_element_type=jnp.float32
    ).astype(jnp.bfloat16)
    direction = jnp.einsum(
        "srk,skn->srn", root_left, product, preferred_element_type=jnp.float32
    )
    square_sums = lax.psum(
        (jnp.sum(adam_step * adam_step, axis=(1, 2)), jnp.sum(direction * direction, axis=(1, 2))),
        "xlo",
    )
    square_sums = lax.psum(square_sums, "z")
    graft = jnp.sqrt(square_sums[0]) / (jnp.sqrt(square_sums[1]) + 1e-06)
    master_new = master - learn_rate * graft[:, None, None] * direction
    occupied_mine = lax.dynamic_slice_in_dim(
        occupied, lax.axis_index("own") * slot_count, slot_count
    )[:, None, None]
    left_next = jnp.where(occupied_mine, left_new, stat_left)
    right_next = jnp.where(occupied_mine, right_new, stat_right)
    master_next = jnp.where(occupied_mine, master_new, master)
    first_next = jnp.where(occupied_mine, first_new, moment_first)
    second_next = jnp.where(occupied_mine, second_new, moment_second)
    shares = master_new.astype(jnp.bfloat16).reshape(
        slot_count, owners, rows_dev // owners, order_size
    )
    delivered = lax.all_to_all(shares, "own", split_axis=1, concat_axis=0, tiled=True)
    delivered = delivered.reshape(owned_slots, rows_dev // owners, order_size)
    weights_out = jnp.take(delivered, owner_map, axis=0)
    return (left_next, right_next, master_next, first_next, second_next, weights_out)


def solution(mesh):
    dp, own = mesh.shape["dp"], mesh.shape["own"]
    split = Mesh(mesh.devices.reshape(dp // 2, 2, own), ("z", "xlo", "own"))
    return jax.shard_map(
        per_device,
        mesh=split,
        in_specs=(
            P(DP, None, "own", None),
            P(),
            P("own", DP, None),
            P("own", DP, None),
            P("own", DP, None),
            P("own", DP, None),
            P("own", DP, None),
            P("own", DP, None),
            P("own", DP, None),
        ),
        out_specs=(
            P("own", DP, None),
            P("own", DP, None),
            P("own", DP, None),
            P("own", DP, None),
            P("own", DP, None),
            P(None, ("z", "xlo", "own"), None),
        ),
        check_vma=False,
    )
```

```python
import jax
import jax.numpy as jnp
from jax import lax
from jax.sharding import Mesh, PartitionSpec as P

stat_decay = 0.9
first_decay = 0.9
second_decay = 0.99
learn_rate = 0.25
DP = ("z", "xlo")


def dp_index():
    return lax.axis_index("z") * lax.axis_size("xlo") + lax.axis_index("xlo")


def dp_gather(x, axis):
    x = lax.all_gather(x, "xlo", axis=axis, tiled=True)
    return lax.all_gather(x, "z", axis=axis, tiled=True)


def dp_sum(x):
    sources = lax.axis_size("z") * lax.axis_size("xlo")
    x = x.reshape(x.shape[0], sources, x.shape[1] // sources, x.shape[2])
    x = lax.all_to_all(x, DP, 1, 1, tiled=True)
    x = jnp.sum(x.astype(jnp.float32), axis=1)
    return dp_gather(x.astype(jnp.bfloat16), 1)


def per_device(
    grads,
    owner_map,
    stat_left,
    stat_right,
    root_left,
    root_right,
    master,
    moment_first,
    moment_second,
):
    owners = lax.axis_size("own")
    slot_count = stat_left.shape[0]
    rows_dev = stat_left.shape[1]
    order_size = stat_left.shape[2]
    blocks = owner_map.shape[0]
    owned_slots = owners * slot_count
    matches = owner_map[:, None] == jnp.arange(owned_slots, dtype=jnp.int32)[None, :]
    occupied = jnp.any(matches, axis=0)
    block_of = jnp.sum(jnp.where(matches, jnp.arange(blocks, dtype=jnp.int32)[:, None], 0), axis=0)
    summed = dp_sum(grads[0].astype(jnp.bfloat16))
    summed, root_right = lax.optimization_barrier((summed, root_right))
    packed = jnp.where(occupied[:, None, None], jnp.take(summed, block_of, axis=0), 0.0)
    packed = packed.reshape(owners, slot_count, summed.shape[1], order_size)
    arrived = lax.all_to_all(packed, "own", split_axis=0, concat_axis=2, tiled=True)
    right_full = dp_gather(root_right, 1)
    first_row = dp_index() * rows_dev
    rounded = arrived.reshape(slot_count, order_size, order_size)
    row_part = lax.dynamic_slice_in_dim(rounded, first_row, rows_dev, 1)
    col_part = lax.dynamic_slice_in_dim(rounded, first_row, rows_dev, 2)
    own_rows = row_part.astype(jnp.float32)
    left_new = stat_decay * stat_left + (1.0 - stat_decay) * jnp.einsum(
        "srk,snk->srn", row_part, rounded, preferred_element_type=jnp.float32
    )
    right_new = stat_decay * stat_right + (1.0 - stat_decay) * jnp.einsum(
        "skr,skn->srn", col_part, rounded, preferred_element_type=jnp.float32
    )
    first_new = first_decay * moment_first + (1.0 - first_decay) * own_rows
    second_new = second_decay * moment_second + (1.0 - second_decay) * own_rows * own_rows
    adam_step = first_new / (jnp.sqrt(second_new) + 1e-08)
    product = jnp.einsum(
        "skn,snr->skr", rounded, right_full, preferred_element_type=jnp.float32
    ).astype(jnp.bfloat16)
    direction = jnp.einsum(
        "srk,skn->srn", root_left, product, preferred_element_type=jnp.float32
    )
    square_sums = lax.psum(
        (jnp.sum(adam_step * adam_step, axis=(1, 2)), jnp.sum(direction * direction, axis=(1, 2))),
        "xlo",
    )
    square_sums = lax.psum(square_sums, "z")
    graft = jnp.sqrt(square_sums[0]) / (jnp.sqrt(square_sums[1]) + 1e-06)
    master_new = master - learn_rate * graft[:, None, None] * direction
    occupied_mine = lax.dynamic_slice_in_dim(
        occupied, lax.axis_index("own") * slot_count, slot_count
    )[:, None, None]
    left_next = jnp.where(occupied_mine, left_new, stat_left)
    right_next = jnp.where(occupied_mine, right_new, stat_right)
    master_next = jnp.where(occupied_mine, master_new, master)
    first_next = jnp.where(occupied_mine, first_new, moment_first)
    second_next = jnp.where(occupied_mine, second_new, moment_second)
    shares = master_new.astype(jnp.bfloat16).reshape(
        slot_count, owners, rows_dev // owners, order_size
    )
    delivered = lax.all_to_all(shares, "own", split_axis=1, concat_axis=0, tiled=True)
    delivered = delivered.reshape(owned_slots, rows_dev // owners, order_size)
    weights_out = jnp.take(delivered, owner_map, axis=0)
    return (left_next, right_next, master_next, first_next, second_next, weights_out)


def solution(mesh):
    dp, own = mesh.shape["dp"], mesh.shape["own"]
    split = Mesh(mesh.devices.reshape(dp // 2, 2, own), ("z", "xlo", "own"))
    return jax.shard_map(
        per_device,
        mesh=split,
        in_specs=(
            P(DP, None, "own", None),
            P(),
            P("own", DP, None),
            P("own", DP, None),
            P("own", DP, None),
            P("own", DP, None),
            P("own", DP, None),
            P("own", DP, None),
            P("own", DP, None),
        ),
        out_specs=(
            P("own", DP, None),
            P("own", DP, None),
            P("own", DP, None),
            P("own", DP, None),
            P("own", DP, None),
            P(None, ("z", "xlo", "own"), None),
        ),
        check_vma=False,
    )
```

```python
import jax
import jax.numpy as jnp
from jax import lax
from jax.sharding import Mesh, PartitionSpec as P

stat_decay = 0.9
first_decay = 0.9
second_decay = 0.99
learn_rate = 0.25
DP = ("z", "xlo")


def dp_index():
    return lax.axis_index("z") * lax.axis_size("xlo") + lax.axis_index("xlo")


def dp_gather(x, axis):
    x = lax.all_gather(x, "xlo", axis=axis, tiled=True)
    return lax.all_gather(x, "z", axis=axis, tiled=True)


def dp_sum(x):
    sources = lax.axis_size("z") * lax.axis_size("xlo")
    x = x.reshape(sources, x.shape[0] // sources, *x.shape[1:])
    x = lax.all_to_all(x, DP, 0, 0, tiled=True)
    return jnp.sum(x.astype(jnp.float32), axis=0).astype(jnp.bfloat16)


def per_device(
    grads,
    owner_map,
    stat_left,
    stat_right,
    root_left,
    root_right,
    master,
    moment_first,
    moment_second,
):
    owners = lax.axis_size("own")
    slot_count = stat_left.shape[0]
    rows_dev = stat_left.shape[1]
    order_size = stat_left.shape[2]
    blocks = owner_map.shape[0]
    owned_slots = owners * slot_count
    matches = owner_map[:, None] == jnp.arange(owned_slots, dtype=jnp.int32)[None, :]
    occupied = jnp.any(matches, axis=0)
    block_of = jnp.sum(jnp.where(matches, jnp.arange(blocks, dtype=jnp.int32)[:, None], 0), axis=0)
    mine = dp_sum(grads[0].astype(jnp.bfloat16))
    chunks = 2
    width = rows_dev // chunks
    arrived = []
    for c in range(chunks):
        summed = dp_gather(mine[:, c * width:(c + 1) * width], 0)
        if c == chunks - 1:
            summed, root_right = lax.optimization_barrier((summed, root_right))
        packed = jnp.where(occupied[:, None, None], jnp.take(summed, block_of, axis=0), 0.0)
        packed = packed.reshape(owners, slot_count, width, order_size)
        piece = lax.all_to_all(packed, "own", split_axis=0, concat_axis=2, tiled=True)
        arrived.append(piece.reshape(slot_count, owners, width, order_size))
    arrived = jnp.stack(arrived, axis=2)
    right_full = dp_gather(root_right, 1)
    first_row = dp_index() * rows_dev
    rounded = arrived.reshape(slot_count, order_size, order_size)
    row_part = lax.dynamic_slice_in_dim(rounded, first_row, rows_dev, 1)
    col_part = lax.dynamic_slice_in_dim(rounded, first_row, rows_dev, 2)
    own_rows = row_part.astype(jnp.float32)
    left_new = stat_decay * stat_left + (1.0 - stat_decay) * jnp.einsum(
        "srk,snk->srn", row_part, rounded, preferred_element_type=jnp.float32
    )
    right_new = stat_decay * stat_right + (1.0 - stat_decay) * jnp.einsum(
        "skr,skn->srn", col_part, rounded, preferred_element_type=jnp.float32
    )
    first_new = first_decay * moment_first + (1.0 - first_decay) * own_rows
    second_new = second_decay * moment_second + (1.0 - second_decay) * own_rows * own_rows
    adam_step = first_new / (jnp.sqrt(second_new) + 1e-08)
    product = jnp.einsum(
        "skn,snr->skr", rounded, right_full, preferred_element_type=jnp.float32
    ).astype(jnp.bfloat16)
    direction = jnp.einsum(
        "srk,skn->srn", root_left, product, preferred_element_type=jnp.float32
    )
    square_sums = lax.psum(
        (jnp.sum(adam_step * adam_step, axis=(1, 2)), jnp.sum(direction * direction, axis=(1, 2))),
        "xlo",
    )
    square_sums = lax.psum(square_sums, "z")
    graft = jnp.sqrt(square_sums[0]) / (jnp.sqrt(square_sums[1]) + 1e-06)
    master_new = master - learn_rate * graft[:, None, None] * direction
    occupied_mine = lax.dynamic_slice_in_dim(
        occupied, lax.axis_index("own") * slot_count, slot_count
    )[:, None, None]
    left_next = jnp.where(occupied_mine, left_new, stat_left)
    right_next = jnp.where(occupied_mine, right_new, stat_right)
    master_next = jnp.where(occupied_mine, master_new, master)
    first_next = jnp.where(occupied_mine, first_new, moment_first)
    second_next = jnp.where(occupied_mine, second_new, moment_second)
    shares = master_new.astype(jnp.bfloat16).reshape(
        slot_count, owners, rows_dev // owners, order_size
    )
    delivered = lax.all_to_all(shares, "own", split_axis=1, concat_axis=0, tiled=True)
    delivered = delivered.reshape(owned_slots, rows_dev // owners, order_size)
    weights_out = jnp.take(delivered, owner_map, axis=0)
    return (left_next, right_next, master_next, first_next, second_next, weights_out)


def solution(mesh):
    dp, own = mesh.shape["dp"], mesh.shape["own"]
    split = Mesh(mesh.devices.reshape(dp // 2, 2, own), ("z", "xlo", "own"))
    return jax.shard_map(
        per_device,
        mesh=split,
        in_specs=(
            P(DP, None, "own", None),
            P(),
            P("own", DP, None),
            P("own", DP, None),
            P("own", DP, None),
            P("own", DP, None),
            P("own", DP, None),
            P("own", DP, None),
            P("own", DP, None),
        ),
        out_specs=(
            P("own", DP, None),
            P("own", DP, None),
            P("own", DP, None),
            P("own", DP, None),
            P("own", DP, None),
            P(None, ("z", "xlo", "own"), None),
        ),
        check_vma=False,
    )
```

```python
import jax
import jax.numpy as jnp
from jax import lax
from jax.sharding import Mesh, PartitionSpec as P

stat_decay = 0.9
first_decay = 0.9
second_decay = 0.99
learn_rate = 0.25
DP = ("z", "xlo")


def dp_index():
    return lax.axis_index("z") * lax.axis_size("xlo") + lax.axis_index("xlo")


def dp_gather(x, axis):
    x = lax.all_gather(x, "xlo", axis=axis, tiled=True)
    return lax.all_gather(x, "z", axis=axis, tiled=True)


def dp_sum(x):
    sources = lax.axis_size("z") * lax.axis_size("xlo")
    x = x.reshape(sources, x.shape[0] // sources, *x.shape[1:])
    x = lax.all_to_all(x, DP, 0, 0, tiled=True)
    return jnp.sum(x.astype(jnp.float32), axis=0).astype(jnp.bfloat16)


def per_device(
    grads,
    owner_map,
    stat_left,
    stat_right,
    root_left,
    root_right,
    master,
    moment_first,
    moment_second,
):
    owners = lax.axis_size("own")
    slot_count = stat_left.shape[0]
    rows_dev = stat_left.shape[1]
    order_size = stat_left.shape[2]
    blocks = owner_map.shape[0]
    owned_slots = owners * slot_count
    matches = owner_map[:, None] == jnp.arange(owned_slots, dtype=jnp.int32)[None, :]
    occupied = jnp.any(matches, axis=0)
    block_of = jnp.sum(jnp.where(matches, jnp.arange(blocks, dtype=jnp.int32)[:, None], 0), axis=0)
    summed = dp_gather(dp_sum(grads[0].astype(jnp.bfloat16)), 0)
    summed, root_right = lax.optimization_barrier((summed, root_right))
    packed = jnp.where(occupied[:, None, None], jnp.take(summed, block_of, axis=0), 0.0)
    packed = packed.reshape(owners, slot_count, rows_dev, order_size)
    arrived = lax.all_to_all(packed, "own", split_axis=0, concat_axis=2, tiled=True)
    right_full = dp_gather(root_right, 1)
    first_row = dp_index() * rows_dev
    rounded = arrived.reshape(slot_count, order_size, order_size)
    row_part = lax.dynamic_slice_in_dim(rounded, first_row, rows_dev, 1)
    col_part = lax.dynamic_slice_in_dim(rounded, first_row, rows_dev, 2)
    own_rows = row_part.astype(jnp.float32)
    left_new = stat_decay * stat_left + (1.0 - stat_decay) * jnp.einsum(
        "srk,snk->srn", row_part, rounded, preferred_element_type=jnp.float32
    )
    right_new = stat_decay * stat_right + (1.0 - stat_decay) * jnp.einsum(
        "skr,skn->srn", col_part, rounded, preferred_element_type=jnp.float32
    )
    first_new = first_decay * moment_first + (1.0 - first_decay) * own_rows
    second_new = second_decay * moment_second + (1.0 - second_decay) * own_rows * own_rows
    adam_step = first_new / (jnp.sqrt(second_new) + 1e-08)
    product = jnp.einsum(
        "skn,snr->skr", rounded, right_full, preferred_element_type=jnp.float32
    ).astype(jnp.bfloat16)
    direction = jnp.einsum(
        "srk,skn->srn", root_left, product, preferred_element_type=jnp.float32
    )
    square_sums = lax.psum(
        (jnp.sum(adam_step * adam_step, axis=(1, 2)), jnp.sum(direction * direction, axis=(1, 2))),
        "xlo",
    )
    square_sums = lax.psum(square_sums, "z")
    graft = jnp.sqrt(square_sums[0]) / (jnp.sqrt(square_sums[1]) + 1e-06)
    master_new = master - learn_rate * graft[:, None, None] * direction
    occupied_mine = lax.dynamic_slice_in_dim(
        occupied, lax.axis_index("own") * slot_count, slot_count
    )[:, None, None]
    left_next = jnp.where(occupied_mine, left_new, stat_left)
    right_next = jnp.where(occupied_mine, right_new, stat_right)
    master_next = jnp.where(occupied_mine, master_new, master)
    first_next = jnp.where(occupied_mine, first_new, moment_first)
    second_next = jnp.where(occupied_mine, second_new, moment_second)
    shares = master_new.astype(jnp.bfloat16).reshape(
        slot_count, owners, rows_dev // owners, order_size
    )
    delivered = lax.all_to_all(shares, "own", split_axis=1, concat_axis=0, tiled=True)
    delivered = delivered.reshape(owned_slots, rows_dev // owners, order_size)
    weights_out = jnp.take(delivered, owner_map, axis=0)
    return (left_next, right_next, master_next, first_next, second_next, weights_out)


def solution(mesh):
    dp, own = mesh.shape["dp"], mesh.shape["own"]
    split = Mesh(mesh.devices.reshape(dp // 2, 2, own), ("z", "xlo", "own"))
    return jax.shard_map(
        per_device,
        mesh=split,
        in_specs=(
            P(DP, None, "own", None),
            P(),
            P("own", DP, None),
            P("own", DP, None),
            P("own", DP, None),
            P("own", DP, None),
            P("own", DP, None),
            P("own", DP, None),
            P("own", DP, None),
        ),
        out_specs=(
            P("own", DP, None),
            P("own", DP, None),
            P("own", DP, None),
            P("own", DP, None),
            P("own", DP, None),
            P(None, ("z", "xlo", "own"), None),
        ),
        check_vma=False,
    )
```

```python
import jax
import jax.numpy as jnp
from jax import lax
from jax.sharding import Mesh, PartitionSpec as P

stat_decay = 0.9
first_decay = 0.9
second_decay = 0.99
learn_rate = 0.25
DP = ("z", "xlo")


def dp_index():
    return lax.axis_index("z") * lax.axis_size("xlo") + lax.axis_index("xlo")


def dp_gather(x, axis):
    x = lax.all_gather(x, "xlo", axis=axis, tiled=True)
    return lax.all_gather(x, "z", axis=axis, tiled=True)


def dp_sum(x):
    sources = lax.axis_size("z") * lax.axis_size("xlo")
    x = x.reshape(sources, x.shape[0] // sources, *x.shape[1:])
    x = lax.all_to_all(x, DP, 0, 0, tiled=True)
    return jnp.sum(x.astype(jnp.float32), axis=0).astype(jnp.bfloat16)


def per_device(
    grads,
    owner_map,
    stat_left,
    stat_right,
    root_left,
    root_right,
    master,
    moment_first,
    moment_second,
):
    owners = lax.axis_size("own")
    slot_count = stat_left.shape[0]
    rows_dev = stat_left.shape[1]
    order_size = stat_left.shape[2]
    blocks = owner_map.shape[0]
    owned_slots = owners * slot_count
    matches = owner_map[:, None] == jnp.arange(owned_slots, dtype=jnp.int32)[None, :]
    occupied = jnp.any(matches, axis=0)
    block_of = jnp.sum(jnp.where(matches, jnp.arange(blocks, dtype=jnp.int32)[:, None], 0), axis=0)
    partner = lax.ppermute(root_right, "xlo", [(0, 1), (1, 0)])
    pair = jnp.where(lax.axis_index("xlo") == 0, jnp.stack([root_right, partner]), jnp.stack([partner, root_right]))
    pair = jnp.swapaxes(pair, 0, 1).reshape(slot_count, 2 * rows_dev, order_size)
    summed = dp_gather(dp_sum(grads[0].astype(jnp.bfloat16)), 0)
    summed, pair = lax.optimization_barrier((summed, pair))
    packed = jnp.take(summed, block_of, axis=0)
    packed = packed.reshape(owners, slot_count, rows_dev, order_size)
    arrived = lax.all_to_all(packed, "own", split_axis=0, concat_axis=2, tiled=True)
    right_full = lax.all_gather(pair, "z", axis=1, tiled=True)
    first_row = dp_index() * rows_dev
    rounded = arrived.reshape(slot_count, order_size, order_size)
    row_part = lax.dynamic_slice_in_dim(rounded, first_row, rows_dev, 1)
    col_part = lax.dynamic_slice_in_dim(rounded, first_row, rows_dev, 2)
    own_rows = row_part.astype(jnp.float32)
    left_new = stat_decay * stat_left + (1.0 - stat_decay) * jnp.einsum(
        "srk,snk->srn", row_part, rounded, preferred_element_type=jnp.float32
    )
    right_new = stat_decay * stat_right + (1.0 - stat_decay) * jnp.einsum(
        "skr,skn->srn", col_part, rounded, preferred_element_type=jnp.float32
    )
    first_new = first_decay * moment_first + (1.0 - first_decay) * own_rows
    second_new = second_decay * moment_second + (1.0 - second_decay) * own_rows * own_rows
    adam_step = first_new / (jnp.sqrt(second_new) + 1e-08)
    product = jnp.einsum(
        "skn,snr->skr", rounded, right_full, preferred_element_type=jnp.float32
    ).astype(jnp.bfloat16)
    direction = jnp.einsum(
        "srk,skn->srn", root_left, product, preferred_element_type=jnp.float32
    )
    square_sums = lax.psum(
        (jnp.sum(adam_step * adam_step, axis=(1, 2)), jnp.sum(direction * direction, axis=(1, 2))),
        "xlo",
    )
    square_sums = lax.psum(square_sums, "z")
    graft = jnp.sqrt(square_sums[0]) / (jnp.sqrt(square_sums[1]) + 1e-06)
    master_new = master - learn_rate * graft[:, None, None] * direction
    occupied_mine = lax.dynamic_slice_in_dim(
        occupied, lax.axis_index("own") * slot_count, slot_count
    )[:, None, None]
    left_next = jnp.where(occupied_mine, left_new, stat_left)
    right_next = jnp.where(occupied_mine, right_new, stat_right)
    master_next = jnp.where(occupied_mine, master_new, master)
    first_next = jnp.where(occupied_mine, first_new, moment_first)
    second_next = jnp.where(occupied_mine, second_new, moment_second)
    shares = master_new.astype(jnp.bfloat16).reshape(
        slot_count, owners, rows_dev // owners, order_size
    )
    delivered = lax.all_to_all(shares, "own", split_axis=1, concat_axis=0, tiled=True)
    delivered = delivered.reshape(owned_slots, rows_dev // owners, order_size)
    weights_out = jnp.take(delivered, owner_map, axis=0)
    return (left_next, right_next, master_next, first_next, second_next, weights_out)


def solution(mesh):
    dp, own = mesh.shape["dp"], mesh.shape["own"]
    split = Mesh(mesh.devices.reshape(dp // 2, 2, own), ("z", "xlo", "own"))
    return jax.shard_map(
        per_device,
        mesh=split,
        in_specs=(
            P(DP, None, "own", None),
            P(),
            P("own", DP, None),
            P("own", DP, None),
            P("own", DP, None),
            P("own", DP, None),
            P("own", DP, None),
            P("own", DP, None),
            P("own", DP, None),
        ),
        out_specs=(
            P("own", DP, None),
            P("own", DP, None),
            P("own", DP, None),
            P("own", DP, None),
            P("own", DP, None),
            P(None, ("z", "xlo", "own"), None),
        ),
        check_vma=False,
    )
```

```python
import jax
import jax.numpy as jnp
from jax import lax
from jax.sharding import Mesh, PartitionSpec as P

stat_decay = 0.9
first_decay = 0.9
second_decay = 0.99
learn_rate = 0.25
DP = ("z", "xlo")


def dp_index():
    return lax.axis_index("z") * lax.axis_size("xlo") + lax.axis_index("xlo")


def dp_gather(x, axis):
    x = lax.all_gather(x, "xlo", axis=axis, tiled=True)
    return lax.all_gather(x, "z", axis=axis, tiled=True)


def dp_sum(x):
    pairs, peers = lax.axis_size("z"), lax.axis_size("xlo")
    x = x.reshape(pairs, peers, x.shape[0] // (pairs * peers), *x.shape[1:])
    x = lax.all_to_all(x, "xlo", 1, 1, tiled=True)
    x = jnp.sum(x.astype(jnp.float32), axis=1).astype(jnp.bfloat16)
    x = lax.all_to_all(x, "z", 0, 0, tiled=True)
    return jnp.sum(x.astype(jnp.float32), axis=0).astype(jnp.bfloat16)


def per_device(
    grads,
    owner_map,
    stat_left,
    stat_right,
    root_left,
    root_right,
    master,
    moment_first,
    moment_second,
):
    owners = lax.axis_size("own")
    slot_count = stat_left.shape[0]
    rows_dev = stat_left.shape[1]
    order_size = stat_left.shape[2]
    blocks = owner_map.shape[0]
    owned_slots = owners * slot_count
    matches = owner_map[:, None] == jnp.arange(owned_slots, dtype=jnp.int32)[None, :]
    occupied = jnp.any(matches, axis=0)
    block_of = jnp.sum(jnp.where(matches, jnp.arange(blocks, dtype=jnp.int32)[:, None], 0), axis=0)
    partner = lax.ppermute(root_right, "xlo", [(0, 1), (1, 0)])
    pair = jnp.where(lax.axis_index("xlo") == 0, jnp.stack([root_right, partner]), jnp.stack([partner, root_right]))
    pair = jnp.swapaxes(pair, 0, 1).reshape(slot_count, 2 * rows_dev, order_size)
    summed = dp_gather(dp_sum(grads[0].astype(jnp.bfloat16)), 0)
    summed, pair = lax.optimization_barrier((summed, pair))
    packed = jnp.take(summed, block_of, axis=0, mode="clip")
    packed = packed.reshape(owners, slot_count, rows_dev, order_size)
    arrived = lax.all_to_all(packed, "own", split_axis=0, concat_axis=2, tiled=True)
    right_full = lax.all_gather(pair, "z", axis=1, tiled=True)
    first_row = dp_index() * rows_dev
    rounded = arrived.reshape(slot_count, order_size, order_size)
    row_part = lax.dynamic_slice_in_dim(rounded, first_row, rows_dev, 1)
    col_part = lax.dynamic_slice_in_dim(rounded, first_row, rows_dev, 2)
    own_rows = row_part.astype(jnp.float32)
    left_new = stat_decay * stat_left + (1.0 - stat_decay) * jnp.einsum(
        "srk,snk->srn", row_part, rounded, preferred_element_type=jnp.float32
    )
    right_new = stat_decay * stat_right + (1.0 - stat_decay) * jnp.einsum(
        "skr,skn->srn", col_part, rounded, preferred_element_type=jnp.float32
    )
    first_new = first_decay * moment_first + (1.0 - first_decay) * own_rows
    second_new = second_decay * moment_second + (1.0 - second_decay) * own_rows * own_rows
    adam_step = first_new / (jnp.sqrt(second_new) + 1e-08)
    product = jnp.einsum(
        "skn,snr->skr", rounded, right_full, preferred_element_type=jnp.float32
    ).astype(jnp.bfloat16)
    direction = jnp.einsum(
        "srk,skn->srn", root_left, product, preferred_element_type=jnp.float32
    )
    square_sums = lax.psum(
        (jnp.sum(adam_step * adam_step, axis=(1, 2)), jnp.sum(direction * direction, axis=(1, 2))),
        "xlo",
    )
    square_sums = lax.psum(square_sums, "z")
    graft = jnp.sqrt(square_sums[0]) / (jnp.sqrt(square_sums[1]) + 1e-06)
    master_new = master - learn_rate * graft[:, None, None] * direction
    occupied_mine = lax.dynamic_slice_in_dim(
        occupied, lax.axis_index("own") * slot_count, slot_count
    )[:, None, None]
    left_next = jnp.where(occupied_mine, left_new, stat_left)
    right_next = jnp.where(occupied_mine, right_new, stat_right)
    master_next = jnp.where(occupied_mine, master_new, master)
    first_next = jnp.where(occupied_mine, first_new, moment_first)
    second_next = jnp.where(occupied_mine, second_new, moment_second)
    shares = master_new.astype(jnp.bfloat16).reshape(
        slot_count, owners, rows_dev // owners, order_size
    )
    delivered = lax.all_to_all(shares, "own", split_axis=1, concat_axis=0, tiled=True)
    delivered = delivered.reshape(owned_slots, rows_dev // owners, order_size)
    weights_out = jnp.take(delivered, owner_map, axis=0, mode="clip")
    return (left_next, right_next, master_next, first_next, second_next, weights_out)


def solution(mesh):
    dp, own = mesh.shape["dp"], mesh.shape["own"]
    split = Mesh(mesh.devices.reshape(dp // 2, 2, own), ("z", "xlo", "own"))
    return jax.shard_map(
        per_device,
        mesh=split,
        in_specs=(
            P(DP, None, "own", None),
            P(),
            P("own", DP, None),
            P("own", DP, None),
            P("own", DP, None),
            P("own", DP, None),
            P("own", DP, None),
            P("own", DP, None),
            P("own", DP, None),
        ),
        out_specs=(
            P("own", DP, None),
            P("own", DP, None),
            P("own", DP, None),
            P("own", DP, None),
            P("own", DP, None),
            P(None, ("z", "xlo", "own"), None),
        ),
        check_vma=False,
    )
```

```python
import jax
import jax.numpy as jnp
from jax import lax
from jax.sharding import Mesh, PartitionSpec as P

stat_decay = 0.9
first_decay = 0.9
second_decay = 0.99
learn_rate = 0.25
DP = ("z", "xlo")


def dp_index():
    return lax.axis_index("z") * lax.axis_size("xlo") + lax.axis_index("xlo")


def dp_gather(x, axis):
    x = lax.all_gather(x, "xlo", axis=axis, tiled=True)
    return lax.all_gather(x, "z", axis=axis, tiled=True)


def dp_sum(x):
    sources = lax.axis_size("z") * lax.axis_size("xlo")
    x = x.reshape(sources, x.shape[0] // sources, *x.shape[1:])
    x = lax.all_to_all(x, DP, 0, 0, tiled=True)
    return jnp.sum(x.astype(jnp.float32), axis=0).astype(jnp.bfloat16)


def per_device(
    grads,
    owner_map,
    stat_left,
    stat_right,
    root_left,
    root_right,
    master,
    moment_first,
    moment_second,
):
    owners = lax.axis_size("own")
    slot_count = stat_left.shape[0]
    rows_dev = stat_left.shape[1]
    order_size = stat_left.shape[2]
    blocks = owner_map.shape[0]
    owned_slots = owners * slot_count
    matches = owner_map[:, None] == jnp.arange(owned_slots, dtype=jnp.int32)[None, :]
    occupied = jnp.any(matches, axis=0)
    block_of = jnp.sum(jnp.where(matches, jnp.arange(blocks, dtype=jnp.int32)[:, None], 0), axis=0)
    partner = lax.ppermute(root_right, "xlo", [(0, 1), (1, 0)])
    pair = jnp.where(lax.axis_index("xlo") == 0, jnp.stack([root_right, partner]), jnp.stack([partner, root_right]))
    pair = jnp.swapaxes(pair, 0, 1).reshape(slot_count, 2 * rows_dev, order_size)
    summed = dp_gather(dp_sum(grads[0].astype(jnp.bfloat16)), 0)
    summed, pair = lax.optimization_barrier((summed, pair))
    packed = jnp.take(summed, block_of, axis=0, mode="clip")
    packed = packed.reshape(owners, slot_count, rows_dev, order_size)
    arrived = lax.all_to_all(packed, "own", split_axis=0, concat_axis=2, tiled=True)
    right_full = lax.all_gather(pair, "z", axis=1, tiled=True)
    first_row = dp_index() * rows_dev
    rounded = arrived.reshape(slot_count, order_size, order_size)
    row_part = lax.dynamic_slice_in_dim(rounded, first_row, rows_dev, 1)
    col_part = lax.dynamic_slice_in_dim(rounded, first_row, rows_dev, 2)
    own_rows = row_part.astype(jnp.float32)
    left_new = stat_decay * stat_left + (1.0 - stat_decay) * jnp.einsum(
        "srk,snk->srn", row_part, rounded, preferred_element_type=jnp.float32
    )
    right_new = stat_decay * stat_right + (1.0 - stat_decay) * jnp.einsum(
        "skr,skn->srn", col_part, rounded, preferred_element_type=jnp.float32
    )
    first_new = first_decay * moment_first + (1.0 - first_decay) * own_rows
    second_new = second_decay * moment_second + (1.0 - second_decay) * own_rows * own_rows
    adam_step = first_new / (jnp.sqrt(second_new) + 1e-08)
    product = jnp.einsum(
        "skn,snr->skr", rounded, right_full, preferred_element_type=jnp.float32
    ).astype(jnp.bfloat16)
    direction = jnp.einsum(
        "srk,skn->srn", root_left, product, preferred_element_type=jnp.float32
    )
    square_sums = lax.psum(
        (jnp.sum(adam_step * adam_step, axis=(1, 2)), jnp.sum(direction * direction, axis=(1, 2))),
        "xlo",
    )
    square_sums = lax.psum(square_sums, "z")
    graft = jnp.sqrt(square_sums[0]) / (jnp.sqrt(square_sums[1]) + 1e-06)
    master_new = master - learn_rate * graft[:, None, None] * direction
    occupied_mine = lax.dynamic_slice_in_dim(
        occupied, lax.axis_index("own") * slot_count, slot_count
    )[:, None, None]
    left_next = jnp.where(occupied_mine, left_new, stat_left)
    right_next = jnp.where(occupied_mine, right_new, stat_right)
    master_next = jnp.where(occupied_mine, master_new, master)
    first_next = jnp.where(occupied_mine, first_new, moment_first)
    second_next = jnp.where(occupied_mine, second_new, moment_second)
    shares = master_new.astype(jnp.bfloat16).reshape(
        slot_count, owners, rows_dev // owners, order_size
    )
    delivered = lax.all_to_all(shares, "own", split_axis=1, concat_axis=0, tiled=True)
    delivered = delivered.reshape(owned_slots, rows_dev // owners, order_size)
    weights_out = jnp.take(delivered, owner_map, axis=0, mode="clip")
    return (left_next, right_next, master_next, first_next, second_next, weights_out)


def solution(mesh):
    dp, own = mesh.shape["dp"], mesh.shape["own"]
    split = Mesh(mesh.devices.reshape(dp // 2, 2, own), ("z", "xlo", "own"))
    return jax.shard_map(
        per_device,
        mesh=split,
        in_specs=(
            P(DP, None, "own", None),
            P(),
            P("own", DP, None),
            P("own", DP, None),
            P("own", DP, None),
            P("own", DP, None),
            P("own", DP, None),
            P("own", DP, None),
            P("own", DP, None),
        ),
        out_specs=(
            P("own", DP, None),
            P("own", DP, None),
            P("own", DP, None),
            P("own", DP, None),
            P("own", DP, None),
            P(None, ("z", "xlo", "own"), None),
        ),
        check_vma=False,
    )
```

```python
import jax
import jax.numpy as jnp
from jax import lax
from jax.sharding import Mesh, PartitionSpec as P

stat_decay = 0.9
first_decay = 0.9
second_decay = 0.99
learn_rate = 0.25
DP = ("z", "xlo")


def dp_index():
    return lax.axis_index("z") * lax.axis_size("xlo") + lax.axis_index("xlo")


def dp_gather(x, axis):
    x = lax.all_gather(x, "xlo", axis=axis, tiled=True)
    return lax.all_gather(x, "z", axis=axis, tiled=True)


def dp_sum(x):
    sources = lax.axis_size("z") * lax.axis_size("xlo")
    x = x.reshape(sources, x.shape[0] // sources, *x.shape[1:])
    x = lax.all_to_all(x, DP, 0, 0, tiled=True)
    return jnp.sum(x.astype(jnp.float32), axis=0).astype(jnp.bfloat16)


def dp_total(x):
    x = x + lax.ppermute(x, "xlo", [(0, 1), (1, 0)])
    ring = lax.axis_size("z")
    step = 1
    while step < ring:
        x = x + lax.ppermute(x, "z", [(i, i ^ step) for i in range(ring)])
        step *= 2
    return x


def per_device(
    grads,
    owner_map,
    stat_left,
    stat_right,
    root_left,
    root_right,
    master,
    moment_first,
    moment_second,
):
    owners = lax.axis_size("own")
    slot_count = stat_left.shape[0]
    rows_dev = stat_left.shape[1]
    order_size = stat_left.shape[2]
    blocks = owner_map.shape[0]
    owned_slots = owners * slot_count
    matches = owner_map[:, None] == jnp.arange(owned_slots, dtype=jnp.int32)[None, :]
    occupied = jnp.any(matches, axis=0)
    block_of = jnp.sum(jnp.where(matches, jnp.arange(blocks, dtype=jnp.int32)[:, None], 0), axis=0)
    partner = lax.ppermute(root_right, "xlo", [(0, 1), (1, 0)])
    pair = jnp.where(lax.axis_index("xlo") == 0, jnp.stack([root_right, partner]), jnp.stack([partner, root_right]))
    pair = jnp.swapaxes(pair, 0, 1).reshape(slot_count, 2 * rows_dev, order_size)
    summed = dp_gather(dp_sum(grads[0].astype(jnp.bfloat16)), 0)
    summed, pair = lax.optimization_barrier((summed, pair))
    packed = jnp.take(summed, block_of, axis=0, mode="clip")
    packed = packed.reshape(owners, slot_count, rows_dev, order_size)
    arrived = lax.all_to_all(packed, "own", split_axis=0, concat_axis=2, tiled=True)
    right_full = lax.all_gather(pair, "z", axis=1, tiled=True)
    first_row = dp_index() * rows_dev
    rounded = arrived.reshape(slot_count, order_size, order_size)
    row_part = lax.dynamic_slice_in_dim(rounded, first_row, rows_dev, 1)
    col_part = lax.dynamic_slice_in_dim(rounded, first_row, rows_dev, 2)
    own_rows = row_part.astype(jnp.float32)
    left_new = stat_decay * stat_left + (1.0 - stat_decay) * jnp.einsum(
        "srk,snk->srn", row_part, rounded, preferred_element_type=jnp.float32
    )
    right_new = stat_decay * stat_right + (1.0 - stat_decay) * jnp.einsum(
        "skr,skn->srn", col_part, rounded, preferred_element_type=jnp.float32
    )
    first_new = first_decay * moment_first + (1.0 - first_decay) * own_rows
    second_new = second_decay * moment_second + (1.0 - second_decay) * own_rows * own_rows
    adam_step = first_new / (jnp.sqrt(second_new) + 1e-08)
    product = jnp.einsum(
        "skn,snr->skr", rounded, right_full, preferred_element_type=jnp.float32
    ).astype(jnp.bfloat16)
    direction = jnp.einsum(
        "srk,skn->srn", root_left, product, preferred_element_type=jnp.float32
    )
    square_sums = dp_total(
        jnp.stack([jnp.sum(adam_step * adam_step, axis=(1, 2)), jnp.sum(direction * direction, axis=(1, 2))])
    )
    graft = jnp.sqrt(square_sums[0]) / (jnp.sqrt(square_sums[1]) + 1e-06)
    master_new = master - learn_rate * graft[:, None, None] * direction
    occupied_mine = lax.dynamic_slice_in_dim(
        occupied, lax.axis_index("own") * slot_count, slot_count
    )[:, None, None]
    left_next = jnp.where(occupied_mine, left_new, stat_left)
    right_next = jnp.where(occupied_mine, right_new, stat_right)
    master_next = jnp.where(occupied_mine, master_new, master)
    first_next = jnp.where(occupied_mine, first_new, moment_first)
    second_next = jnp.where(occupied_mine, second_new, moment_second)
    shares = master_new.astype(jnp.bfloat16).reshape(
        slot_count, owners, rows_dev // owners, order_size
    )
    delivered = lax.all_to_all(shares, "own", split_axis=1, concat_axis=0, tiled=True)
    delivered = delivered.reshape(owned_slots, rows_dev // owners, order_size)
    weights_out = jnp.take(delivered, owner_map, axis=0, mode="clip")
    return (left_next, right_next, master_next, first_next, second_next, weights_out)


def solution(mesh):
    dp, own = mesh.shape["dp"], mesh.shape["own"]
    split = Mesh(mesh.devices.reshape(dp // 2, 2, own), ("z", "xlo", "own"))
    return jax.shard_map(
        per_device,
        mesh=split,
        in_specs=(
            P(DP, None, "own", None),
            P(),
            P("own", DP, None),
            P("own", DP, None),
            P("own", DP, None),
            P("own", DP, None),
            P("own", DP, None),
            P("own", DP, None),
            P("own", DP, None),
        ),
        out_specs=(
            P("own", DP, None),
            P("own", DP, None),
            P("own", DP, None),
            P("own", DP, None),
            P("own", DP, None),
            P(None, ("z", "xlo", "own"), None),
        ),
        check_vma=False,
    )
```

```python
import jax
import jax.numpy as jnp
from jax import lax
from jax.sharding import Mesh, PartitionSpec as P

stat_decay = 0.9
first_decay = 0.9
second_decay = 0.99
learn_rate = 0.25
DP = ("z", "xlo")


def dp_index():
    return lax.axis_index("z") * lax.axis_size("xlo") + lax.axis_index("xlo")


def dp_gather(x, axis):
    x = lax.all_gather(x, "xlo", axis=axis, tiled=True)
    return lax.all_gather(x, "z", axis=axis, tiled=True)


def dp_sum(x):
    sources = lax.axis_size("z") * lax.axis_size("xlo")
    x = x.reshape(sources, x.shape[0] // sources, *x.shape[1:])
    x = lax.all_to_all(x, DP, 0, 0, tiled=True)
    return jnp.sum(x.astype(jnp.float32), axis=0).astype(jnp.bfloat16)


def dp_total(x):
    size = lax.axis_size("z") * lax.axis_size("xlo")
    total = x
    for shift in range(1, size):
        total = total + lax.ppermute(x, DP, [(i, (i + shift) % size) for i in range(size)])
    return total


def per_device(
    grads,
    owner_map,
    stat_left,
    stat_right,
    root_left,
    root_right,
    master,
    moment_first,
    moment_second,
):
    owners = lax.axis_size("own")
    slot_count = stat_left.shape[0]
    rows_dev = stat_left.shape[1]
    order_size = stat_left.shape[2]
    blocks = owner_map.shape[0]
    owned_slots = owners * slot_count
    matches = owner_map[:, None] == jnp.arange(owned_slots, dtype=jnp.int32)[None, :]
    occupied = jnp.any(matches, axis=0)
    block_of = jnp.sum(jnp.where(matches, jnp.arange(blocks, dtype=jnp.int32)[:, None], 0), axis=0)
    partner = lax.ppermute(root_right, "xlo", [(0, 1), (1, 0)])
    pair = jnp.where(lax.axis_index("xlo") == 0, jnp.stack([root_right, partner]), jnp.stack([partner, root_right]))
    pair = jnp.swapaxes(pair, 0, 1).reshape(slot_count, 2 * rows_dev, order_size)
    summed = dp_gather(dp_sum(grads[0].astype(jnp.bfloat16)), 0)
    summed, pair = lax.optimization_barrier((summed, pair))
    packed = jnp.take(summed, block_of, axis=0, mode="clip")
    packed = packed.reshape(owners, slot_count, rows_dev, order_size)
    arrived = lax.all_to_all(packed, "own", split_axis=0, concat_axis=2, tiled=True)
    right_full = lax.all_gather(pair, "z", axis=1, tiled=True)
    first_row = dp_index() * rows_dev
    rounded = arrived.reshape(slot_count, order_size, order_size)
    row_part = lax.dynamic_slice_in_dim(rounded, first_row, rows_dev, 1)
    col_part = lax.dynamic_slice_in_dim(rounded, first_row, rows_dev, 2)
    own_rows = row_part.astype(jnp.float32)
    left_new = stat_decay * stat_left + (1.0 - stat_decay) * jnp.einsum(
        "srk,snk->srn", row_part, rounded, preferred_element_type=jnp.float32
    )
    right_new = stat_decay * stat_right + (1.0 - stat_decay) * jnp.einsum(
        "skr,skn->srn", col_part, rounded, preferred_element_type=jnp.float32
    )
    first_new = first_decay * moment_first + (1.0 - first_decay) * own_rows
    second_new = second_decay * moment_second + (1.0 - second_decay) * own_rows * own_rows
    adam_step = first_new / (jnp.sqrt(second_new) + 1e-08)
    product = jnp.einsum(
        "skn,snr->skr", rounded, right_full, preferred_element_type=jnp.float32
    ).astype(jnp.bfloat16)
    direction = jnp.einsum(
        "srk,skn->srn", root_left, product, preferred_element_type=jnp.float32
    )
    square_sums = dp_total(
        jnp.stack([jnp.sum(adam_step * adam_step, axis=(1, 2)), jnp.sum(direction * direction, axis=(1, 2))])
    )
    graft = jnp.sqrt(square_sums[0]) / (jnp.sqrt(square_sums[1]) + 1e-06)
    master_new = master - learn_rate * graft[:, None, None] * direction
    occupied_mine = lax.dynamic_slice_in_dim(
        occupied, lax.axis_index("own") * slot_count, slot_count
    )[:, None, None]
    left_next = jnp.where(occupied_mine, left_new, stat_left)
    right_next = jnp.where(occupied_mine, right_new, stat_right)
    master_next = jnp.where(occupied_mine, master_new, master)
    first_next = jnp.where(occupied_mine, first_new, moment_first)
    second_next = jnp.where(occupied_mine, second_new, moment_second)
    shares = master_new.astype(jnp.bfloat16).reshape(
        slot_count, owners, rows_dev // owners, order_size
    )
    delivered = lax.all_to_all(shares, "own", split_axis=1, concat_axis=0, tiled=True)
    delivered = delivered.reshape(owned_slots, rows_dev // owners, order_size)
    weights_out = jnp.take(delivered, owner_map, axis=0, mode="clip")
    return (left_next, right_next, master_next, first_next, second_next, weights_out)


def solution(mesh):
    dp, own = mesh.shape["dp"], mesh.shape["own"]
    split = Mesh(mesh.devices.reshape(dp // 2, 2, own), ("z", "xlo", "own"))
    return jax.shard_map(
        per_device,
        mesh=split,
        in_specs=(
            P(DP, None, "own", None),
            P(),
            P("own", DP, None),
            P("own", DP, None),
            P("own", DP, None),
            P("own", DP, None),
            P("own", DP, None),
            P("own", DP, None),
            P("own", DP, None),
        ),
        out_specs=(
            P("own", DP, None),
            P("own", DP, None),
            P("own", DP, None),
            P("own", DP, None),
            P("own", DP, None),
            P(None, ("z", "xlo", "own"), None),
        ),
        check_vma=False,
    )
```

```python
import jax
import jax.numpy as jnp
from jax import lax
from jax.sharding import Mesh, PartitionSpec as P

stat_decay = 0.9
first_decay = 0.9
second_decay = 0.99
learn_rate = 0.25
DP = ("z", "xlo")


def dp_index():
    return lax.axis_index("z") * lax.axis_size("xlo") + lax.axis_index("xlo")


def dp_gather(x, axis):
    x = lax.all_gather(x, "xlo", axis=axis, tiled=True)
    return lax.all_gather(x, "z", axis=axis, tiled=True)


def dp_sum(x):
    sources = lax.axis_size("z") * lax.axis_size("xlo")
    x = x.reshape(sources, x.shape[0] // sources, *x.shape[1:])
    x = lax.all_to_all(x, DP, 0, 0, tiled=True)
    return jnp.sum(x.astype(jnp.float32), axis=0).astype(jnp.bfloat16)


def dp_total(x, later):
    x = x + lax.ppermute(x, "xlo", [(0, 1), (1, 0)])
    x, later = lax.optimization_barrier((x, later))
    ring = lax.axis_size("z")
    step = 1
    while step < ring:
        x = x + lax.ppermute(x, "z", [(i, i ^ step) for i in range(ring)])
        step *= 2
    return x, later


def per_device(
    grads,
    owner_map,
    stat_left,
    stat_right,
    root_left,
    root_right,
    master,
    moment_first,
    moment_second,
):
    owners = lax.axis_size("own")
    slot_count = stat_left.shape[0]
    rows_dev = stat_left.shape[1]
    order_size = stat_left.shape[2]
    blocks = owner_map.shape[0]
    owned_slots = owners * slot_count
    matches = owner_map[:, None] == jnp.arange(owned_slots, dtype=jnp.int32)[None, :]
    occupied = jnp.any(matches, axis=0)
    block_of = jnp.sum(jnp.where(matches, jnp.arange(blocks, dtype=jnp.int32)[:, None], 0), axis=0)
    partner = lax.ppermute(root_right, "xlo", [(0, 1), (1, 0)])
    pair = jnp.where(lax.axis_index("xlo") == 0, jnp.stack([root_right, partner]), jnp.stack([partner, root_right]))
    pair = jnp.swapaxes(pair, 0, 1).reshape(slot_count, 2 * rows_dev, order_size)
    summed = dp_gather(dp_sum(grads[0].astype(jnp.bfloat16)), 0)
    summed, pair = lax.optimization_barrier((summed, pair))
    packed = jnp.take(summed, block_of, axis=0, mode="clip")
    packed = packed.reshape(owners, slot_count, rows_dev, order_size)
    arrived = lax.all_to_all(packed, "own", split_axis=0, concat_axis=2, tiled=True)
    right_full = lax.all_gather(pair, "z", axis=1, tiled=True)
    first_row = dp_index() * rows_dev
    rounded = arrived.reshape(slot_count, order_size, order_size)
    row_part = lax.dynamic_slice_in_dim(rounded, first_row, rows_dev, 1)
    col_part = lax.dynamic_slice_in_dim(rounded, first_row, rows_dev, 2)
    own_rows = row_part.astype(jnp.float32)
    first_new = first_decay * moment_first + (1.0 - first_decay) * own_rows
    second_new = second_decay * moment_second + (1.0 - second_decay) * own_rows * own_rows
    adam_step = first_new / (jnp.sqrt(second_new) + 1e-08)
    product = jnp.einsum(
        "skn,snr->skr", rounded, right_full, preferred_element_type=jnp.float32
    ).astype(jnp.bfloat16)
    direction = jnp.einsum(
        "srk,skn->srn", root_left, product, preferred_element_type=jnp.float32
    )
    square_sums, (row_late, col_late, rounded_late) = dp_total(
        jnp.stack([jnp.sum(adam_step * adam_step, axis=(1, 2)), jnp.sum(direction * direction, axis=(1, 2))]),
        (row_part, col_part, rounded),
    )
    left_new = stat_decay * stat_left + (1.0 - stat_decay) * jnp.einsum(
        "srk,snk->srn", row_late, rounded_late, preferred_element_type=jnp.float32
    )
    right_new = stat_decay * stat_right + (1.0 - stat_decay) * jnp.einsum(
        "skr,skn->srn", col_late, rounded_late, preferred_element_type=jnp.float32
    )
    graft = jnp.sqrt(square_sums[0]) / (jnp.sqrt(square_sums[1]) + 1e-06)
    master_new = master - learn_rate * graft[:, None, None] * direction
    occupied_mine = lax.dynamic_slice_in_dim(
        occupied, lax.axis_index("own") * slot_count, slot_count
    )[:, None, None]
    left_next = jnp.where(occupied_mine, left_new, stat_left)
    right_next = jnp.where(occupied_mine, right_new, stat_right)
    master_next = jnp.where(occupied_mine, master_new, master)
    first_next = jnp.where(occupied_mine, first_new, moment_first)
    second_next = jnp.where(occupied_mine, second_new, moment_second)
    shares = master_new.astype(jnp.bfloat16).reshape(
        slot_count, owners, rows_dev // owners, order_size
    )
    delivered = lax.all_to_all(shares, "own", split_axis=1, concat_axis=0, tiled=True)
    delivered = delivered.reshape(owned_slots, rows_dev // owners, order_size)
    weights_out = jnp.take(delivered, owner_map, axis=0, mode="clip")
    return (left_next, right_next, master_next, first_next, second_next, weights_out)


def solution(mesh):
    dp, own = mesh.shape["dp"], mesh.shape["own"]
    split = Mesh(mesh.devices.reshape(dp // 2, 2, own), ("z", "xlo", "own"))
    return jax.shard_map(
        per_device,
        mesh=split,
        in_specs=(
            P(DP, None, "own", None),
            P(),
            P("own", DP, None),
            P("own", DP, None),
            P("own", DP, None),
            P("own", DP, None),
            P("own", DP, None),
            P("own", DP, None),
            P("own", DP, None),
        ),
        out_specs=(
            P("own", DP, None),
            P("own", DP, None),
            P("own", DP, None),
            P("own", DP, None),
            P("own", DP, None),
            P(None, ("z", "xlo", "own"), None),
        ),
        check_vma=False,
    )
```

```python
import jax
import jax.numpy as jnp
from jax import lax
from jax.sharding import Mesh, PartitionSpec as P

stat_decay = 0.9
first_decay = 0.9
second_decay = 0.99
learn_rate = 0.25
DP = ("z", "xlo")


def dp_index():
    return lax.axis_index("z") * lax.axis_size("xlo") + lax.axis_index("xlo")


def dp_gather(x, axis):
    x = lax.all_gather(x, "xlo", axis=axis, tiled=True)
    return lax.all_gather(x, "z", axis=axis, tiled=True)


def dp_sum(x):
    pairs, peers = lax.axis_size("z"), lax.axis_size("xlo")
    x = x.reshape(peers, pairs, x.shape[0] // (pairs * peers), *x.shape[1:])
    x = jnp.swapaxes(x, 0, 1).reshape(pairs * peers, -1, *x.shape[3:])
    x = lax.all_to_all(x, DP, 0, 0, tiled=True)
    return jnp.sum(x.astype(jnp.float32), axis=0).astype(jnp.bfloat16)


def block_gather(x):
    x = lax.all_gather(x, "z", axis=0, tiled=True)
    return lax.all_gather(x, "xlo", axis=0, tiled=True)


def dp_total(x):
    x = x + lax.ppermute(x, "xlo", [(0, 1), (1, 0)])
    ring = lax.axis_size("z")
    step = 1
    while step < ring:
        x = x + lax.ppermute(x, "z", [(i, i ^ step) for i in range(ring)])
        step *= 2
    return x


def per_device(
    grads,
    owner_map,
    stat_left,
    stat_right,
    root_left,
    root_right,
    master,
    moment_first,
    moment_second,
):
    owners = lax.axis_size("own")
    slot_count = stat_left.shape[0]
    rows_dev = stat_left.shape[1]
    order_size = stat_left.shape[2]
    blocks = owner_map.shape[0]
    owned_slots = owners * slot_count
    matches = owner_map[:, None] == jnp.arange(owned_slots, dtype=jnp.int32)[None, :]
    occupied = jnp.any(matches, axis=0)
    block_of = jnp.sum(jnp.where(matches, jnp.arange(blocks, dtype=jnp.int32)[:, None], 0), axis=0)
    partner = lax.ppermute(root_right, "xlo", [(0, 1), (1, 0)])
    pair = jnp.where(lax.axis_index("xlo") == 0, jnp.stack([root_right, partner]), jnp.stack([partner, root_right]))
    pair = jnp.swapaxes(pair, 0, 1).reshape(slot_count, 2 * rows_dev, order_size)
    summed = block_gather(dp_sum(grads[0].astype(jnp.bfloat16)))
    summed, pair = lax.optimization_barrier((summed, pair))
    packed = jnp.take(summed, block_of, axis=0, mode="clip")
    packed = packed.reshape(owners, slot_count, rows_dev, order_size)
    arrived = lax.all_to_all(packed, "own", split_axis=0, concat_axis=2, tiled=True)
    right_full = lax.all_gather(pair, "z", axis=1, tiled=True)
    first_row = dp_index() * rows_dev
    rounded = arrived.reshape(slot_count, order_size, order_size)
    row_part = lax.dynamic_slice_in_dim(rounded, first_row, rows_dev, 1)
    col_part = lax.dynamic_slice_in_dim(rounded, first_row, rows_dev, 2)
    own_rows = row_part.astype(jnp.float32)
    left_new = stat_decay * stat_left + (1.0 - stat_decay) * jnp.einsum(
        "srk,snk->srn", row_part, rounded, preferred_element_type=jnp.float32
    )
    right_new = stat_decay * stat_right + (1.0 - stat_decay) * jnp.einsum(
        "skr,skn->srn", col_part, rounded, preferred_element_type=jnp.float32
    )
    first_new = first_decay * moment_first + (1.0 - first_decay) * own_rows
    second_new = second_decay * moment_second + (1.0 - second_decay) * own_rows * own_rows
    adam_step = first_new / (jnp.sqrt(second_new) + 1e-08)
    product = jnp.einsum(
        "skn,snr->skr", rounded, right_full, preferred_element_type=jnp.float32
    ).astype(jnp.bfloat16)
    direction = jnp.einsum(
        "srk,skn->srn", root_left, product, preferred_element_type=jnp.float32
    )
    square_sums = dp_total(
        jnp.stack([jnp.sum(adam_step * adam_step, axis=(1, 2)), jnp.sum(direction * direction, axis=(1, 2))])
    )
    graft = jnp.sqrt(square_sums[0]) / (jnp.sqrt(square_sums[1]) + 1e-06)
    master_new = master - learn_rate * graft[:, None, None] * direction
    occupied_mine = lax.dynamic_slice_in_dim(
        occupied, lax.axis_index("own") * slot_count, slot_count
    )[:, None, None]
    left_next = jnp.where(occupied_mine, left_new, stat_left)
    right_next = jnp.where(occupied_mine, right_new, stat_right)
    master_next = jnp.where(occupied_mine, master_new, master)
    first_next = jnp.where(occupied_mine, first_new, moment_first)
    second_next = jnp.where(occupied_mine, second_new, moment_second)
    shares = master_new.astype(jnp.bfloat16).reshape(
        slot_count, owners, rows_dev // owners, order_size
    )
    delivered = lax.all_to_all(shares, "own", split_axis=1, concat_axis=0, tiled=True)
    delivered = delivered.reshape(owned_slots, rows_dev // owners, order_size)
    weights_out = jnp.take(delivered, owner_map, axis=0, mode="clip")
    return (left_next, right_next, master_next, first_next, second_next, weights_out)


def solution(mesh):
    dp, own = mesh.shape["dp"], mesh.shape["own"]
    split = Mesh(mesh.devices.reshape(dp // 2, 2, own), ("z", "xlo", "own"))
    return jax.shard_map(
        per_device,
        mesh=split,
        in_specs=(
            P(DP, None, "own", None),
            P(),
            P("own", DP, None),
            P("own", DP, None),
            P("own", DP, None),
            P("own", DP, None),
            P("own", DP, None),
            P("own", DP, None),
            P("own", DP, None),
        ),
        out_specs=(
            P("own", DP, None),
            P("own", DP, None),
            P("own", DP, None),
            P("own", DP, None),
            P("own", DP, None),
            P(None, ("z", "xlo", "own"), None),
        ),
        check_vma=False,
    )
```
